256 devices in a mesh: rep: 16 (over x, y_lo, core), blk: 16 (over y_hi, z).
Axes of the slice: x: 4, y: 4 (y_hi: 2, y_lo: 2; y = y_hi * 2 + y_lo), z: 8, core: 2. Of those that a mesh axis runs over, the one named last changes fastest.
Arguments:
- features: bfloat16 [65536, 1024], P(('rep', 'blk')), may hold values from -6 to 6
- weight: bfloat16 [1024, 1024], replicated, may hold values from -0.1875 to 0.1875
- bias: bfloat16 [1024], replicated, may hold values from -3 to 3
- tile_vals: bfloat16 [16, 16, 32, 4, 128, 128], P('rep', 'blk'), may hold values from -0.125 to 0.125
- tile_col: int32 [16, 16, 32, 4], P('rep', 'blk'), may hold values from 0 to 31
- tile_count: int32 [16, 16, 32], P('rep', 'blk'), may hold values from 0 to 4, as said below
Outputs:
- hidden: bfloat16 [65536, 1024], P(('rep', 'blk'))
The draws below stay inside these ranges and needn't reach their ends.
Inputs may be any that keep to these rules, and one draw needn't show every extreme that they name: The first tile_count slots are the live ones; some entry equals 4 in every draw.
All inputs are finite; a program needn't handle non-finite values.
Results may differ from the reference program's by a relative error of at most 0.014.
Values may be sent and summed in bfloat16 or wider, within the bound.
No kernel may reach another device: no remote copies, remote signals or barrier semaphores. Data moves between devices by JAX's collectives and lax.ppermute only.
A program may use at most 64 MiB of HBM per device.

```python
import jax
import jax.numpy as jnp
from jax import lax

D = 1024
TB = 128
SLOTS = 4
RB_DEV = 2
GROUP_BLOCKS = 32
SOURCE_BLOCKS = 32
NODES = 65536
N_REP = 16
N_BLK = 16


def draw_tile_count(key, part):
    key_level = jax.random.fold_in(key, 11)
    key_other = jax.random.fold_in(key, 12)
    key_count = jax.random.fold_in(key, 13)
    key_spot = jax.random.fold_in(key, 14)
    level_one = jax.random.randint(key_level, (N_REP, N_BLK, 1), 0, SLOTS)
    level_two = jax.random.randint(key_other, (N_REP, N_BLK, 1), 0, SLOTS)
    level = 1 + level_one * level_two // (SLOTS - 1)
    counts = jax.random.randint(key_count, (N_REP, N_BLK, GROUP_BLOCKS), 0, level + 1)
    spot_rep = jax.random.randint(jax.random.fold_in(key_spot, 1), (), 0, N_REP)
    spot_blk = jax.random.randint(jax.random.fold_in(key_spot, 2), (), 0, N_BLK)
    spot_row = jax.random.randint(jax.random.fold_in(key_spot, 3), (), 0, GROUP_BLOCKS)
    counts = counts.at[spot_rep, spot_blk, spot_row].set(SLOTS)
    return counts.astype(jnp.int32)


def plant(drawn, key, smallest, top_value):
    spot = [jax.random.randint(jax.random.fold_in(key, axis), (), 0, length) for axis, length in enumerate(drawn.shape)]
    longest = drawn.shape.index(max(drawn.shape))
    beside = spot[:longest] + [(spot[longest] + 1) % drawn.shape[longest]] + spot[longest + 1:]
    return drawn.at[tuple(spot)].set(smallest).at[tuple(beside)].set(top_value)


def shard_levels(key, extent, cuts, low, top_value):
    def one(position, parts):
        heights = jax.random.uniform(jax.random.fold_in(jax.random.fold_in(key, 6), position), (parts,), jnp.float32, low / len(cuts), top_value / len(cuts))
        return jnp.repeat(jnp.exp(heights), extent[position] // parts).reshape((-1,) + (1,) * (len(extent) - position - 1))

    level = one(*cuts[0])
    for cut in cuts[1:]:
        level = level * one(*cut)
    return level


def scatter_about(own_key, dims, spread, most, shards=(), kind=jnp.bfloat16):
    array = jax.random.normal(own_key, dims, jnp.float32) * spread
    if len(shards) > 0:
        array = shard_levels(own_key, dims, shards, -0.22, 0.18) * array
    return jnp.clip(array, min=-most, max=most).astype(kind)


def setup_inputs(seed: int = 0) -> dict:
    keys = jax.random.split(jax.random.key(seed), 7)
    return {
        "features": scatter_about(keys[0], (NODES, D), 1.0, 6.0, ((0, 256),)),
        "weight": scatter_about(keys[1], (D, D), D ** -0.5, 0.1875),
        "bias": scatter_about(keys[2], (D,), 0.5, 3.0),
        "tile_vals": scatter_about(keys[3], (N_REP, N_BLK, GROUP_BLOCKS, SLOTS, TB, TB), (TB * N_BLK) ** -0.5, 0.125, ((0, 16), (1, 16))),
        "tile_col": plant(jax.random.randint(keys[4], (N_REP, N_BLK, GROUP_BLOCKS, SLOTS), 0, SOURCE_BLOCKS), jax.random.fold_in(keys[4], 1), 0, SOURCE_BLOCKS - 1).astype(jnp.int32),
        "tile_count": draw_tile_count(jax.random.fold_in(keys[6], 71), 0),
    }


def reference(features, weight, bias, tile_vals, tile_col, tile_count):
    feat_five = features.reshape(N_REP, N_BLK, RB_DEV, TB, D)

    def group_rows(inputs):
        group_tiles, group_cols, group_counts = inputs

        def over_slab(accum, slab_inputs):
            slab_id, slab_tiles, slab_cols, slab_counts = slab_inputs
            slab_rows = lax.dynamic_index_in_dim(feat_five, slab_id, 1, keepdims=False)
            slab_rows = slab_rows.reshape(N_REP * RB_DEV, TB, D)
            sources = jnp.take(slab_rows, slab_cols, axis=0).astype(jnp.float32)
            live_mask = (jnp.arange(SLOTS, dtype=jnp.int32)[None, :] < slab_counts[:, None]).astype(jnp.float32)
            masked = slab_tiles.astype(jnp.float32) * live_mask[:, :, None, None]
            partial_value = jnp.einsum("bkij,bkjd->bid", masked, sources).astype(jnp.bfloat16)
            partial_value = lax.optimization_barrier(partial_value)
            return accum + partial_value.astype(jnp.float32), None

        start = jnp.zeros((GROUP_BLOCKS, TB, D), jnp.float32)
        slab_ids = jnp.arange(N_BLK, dtype=jnp.int32)
        accum, unused = lax.scan(over_slab, start, (slab_ids, group_tiles, group_cols, group_counts))
        aggregated = accum.reshape(GROUP_BLOCKS * TB, D).astype(jnp.bfloat16)
        mixed = jnp.dot(aggregated, weight, preferred_element_type=jnp.float32) + bias.astype(jnp.float32)
        return jnp.maximum(mixed, 0.0).astype(jnp.bfloat16)

    outputs = lax.map(group_rows, (tile_vals, tile_col, tile_count))
    return outputs.reshape(NODES, D)
```

```python
import jax
import jax.numpy as jnp
from jax import lax
from jax.experimental import pallas as pl
from jax.experimental.pallas import tpu as pltpu
from jax.sharding import PartitionSpec as P


def sparse_partial(gathered, tiles, cols, counts):
    n_blocks, slots, side, _ = tiles.shape
    width = gathered.shape[1]
    n_src = gathered.shape[0]

    def kernel(cols_ref, counts_ref, tile_ref, src_ref, out_ref, acc_ref):
        b = pl.program_id(0)
        live = counts_ref[b]
        acc_ref[...] = jnp.zeros_like(acc_ref)
        for k in range(slots):
            @pl.when(k < live)
            def _():
                start = pl.multiple_of(cols_ref[b * slots + k] * side, side)
                src = src_ref[pl.ds(start, side), :]
                acc_ref[...] += jnp.dot(tile_ref[0, k], src, preferred_element_type=jnp.float32)
        out_ref[...] = acc_ref[...].astype(out_ref.dtype)

    grid_spec = pltpu.PrefetchScalarGridSpec(
        num_scalar_prefetch=2,
        grid=(n_blocks,),
        in_specs=[
            pl.BlockSpec((1, slots, side, side), lambda b, c, n: (b, 0, 0, 0)),
            pl.BlockSpec((n_src, width), lambda b, c, n: (0, 0)),
        ],
        out_specs=pl.BlockSpec((side, width), lambda b, c, n: (b, 0)),
        scratch_shapes=[pltpu.VMEM((side, width), jnp.float32)],
    )
    return pl.pallas_call(
        kernel,
        grid_spec=grid_spec,
        out_shape=jax.ShapeDtypeStruct((n_blocks * side, width), jnp.bfloat16),
        compiler_params=pltpu.CompilerParams(
            dimension_semantics=("arbitrary",), vmem_limit_bytes=48 * 1024 * 1024
        ),
    )(cols.reshape(-1), counts, tiles, gathered)


def body(features, weight, bias, tile_vals, tile_col, tile_count):
    gathered = lax.all_gather(features, "rep", axis=0, tiled=True)
    partial = sparse_partial(gathered, tile_vals[0, 0], tile_col[0, 0], tile_count[0, 0])
    summed = lax.psum_scatter(partial, "blk", scatter_dimension=0, tiled=True)
    mixed = jnp.dot(summed, weight, preferred_element_type=jnp.float32) + bias.astype(jnp.float32)
    return jnp.maximum(mixed, 0.0).astype(jnp.bfloat16)


def solution(mesh):
    return jax.shard_map(
        body,
        mesh=mesh,
        in_specs=(
            P(("rep", "blk"), None),
            P(),
            P(),
            P("rep", "blk", None, None, None, None),
            P("rep", "blk", None, None),
            P("rep", "blk", None),
        ),
        out_specs=P(("rep", "blk"), None),
        check_vma=False,
    )
```

```python
import jax
import jax.numpy as jnp
from jax import lax
from jax.experimental import pallas as pl
from jax.experimental.pallas import tpu as pltpu
from jax.sharding import Mesh, PartitionSpec as P


def sparse_partial(gathered, tiles, cols, counts, out_pos):
    n_blocks, slots, side, _ = tiles.shape
    width = gathered.shape[1]
    n_src = gathered.shape[0]

    def kernel(cols_ref, counts_ref, tile_ref, src_ref, out_ref, acc_ref):
        b = pl.program_id(0)
        live = counts_ref[b]
        acc_ref[...] = jnp.zeros_like(acc_ref)
        for k in range(slots):
            @pl.when(k < live)
            def _():
                start = pl.multiple_of(cols_ref[b * slots + k] * side, side)
                src = src_ref[pl.ds(start, side), :]
                acc_ref[...] += jnp.dot(tile_ref[0, k], src, preferred_element_type=jnp.float32)
        out_ref[...] = acc_ref[...].astype(out_ref.dtype)

    grid_spec = pltpu.PrefetchScalarGridSpec(
        num_scalar_prefetch=2,
        grid=(n_blocks,),
        in_specs=[
            pl.BlockSpec((1, slots, side, side), lambda b, c, n: (b, 0, 0, 0)),
            pl.BlockSpec((n_src, width), lambda b, c, n: (0, 0)),
        ],
        out_specs=pl.BlockSpec((side, width), lambda b, c, n: (out_pos(b), 0)),
        scratch_shapes=[pltpu.VMEM((side, width), jnp.float32)],
    )
    return pl.pallas_call(
        kernel,
        grid_spec=grid_spec,
        out_shape=jax.ShapeDtypeStruct((n_blocks * side, width), jnp.bfloat16),
        compiler_params=pltpu.CompilerParams(
            dimension_semantics=("arbitrary",), vmem_limit_bytes=48 * 1024 * 1024
        ),
    )(cols.reshape(-1), counts, tiles, gathered)


def body(features, weight, bias, tile_vals, tile_col, tile_count):
    n_hi = lax.axis_size("yh")
    n_lo = lax.axis_size("z")
    per_dev = features.shape[0] // tile_vals.shape[-1]

    def out_pos(b):
        j = b // per_dev
        return ((j % n_lo) * n_hi + j // n_lo) * per_dev + b % per_dev

    gathered = lax.all_gather(features, "rep", axis=0, tiled=True)
    partial = sparse_partial(gathered, tile_vals[0, 0], tile_col[0, 0], tile_count[0, 0], out_pos)
    summed = lax.psum_scatter(partial, "z", scatter_dimension=0, tiled=True)
    summed = lax.psum_scatter(summed, "yh", scatter_dimension=0, tiled=True)
    mixed = jnp.dot(summed, weight, preferred_element_type=jnp.float32) + bias.astype(jnp.float32)
    return jnp.maximum(mixed, 0.0).astype(jnp.bfloat16)


def solution(mesh):
    n_rep, n_blk = mesh.devices.shape
    n_hi = 2
    split = Mesh(mesh.devices.reshape(n_rep, n_hi, n_blk // n_hi), ("rep", "yh", "z"))
    blk = ("yh", "z")
    return jax.shard_map(
        body,
        mesh=split,
        in_specs=(
            P(("rep",) + blk, None),
            P(),
            P(),
            P("rep", blk, None, None, None, None),
            P("rep", blk, None, None),
            P("rep", blk, None),
        ),
        out_specs=P(("rep",) + blk, None),
        check_vma=False,
    )
```

```python
import jax
import jax.numpy as jnp
from jax import lax
from jax.experimental import pallas as pl
from jax.experimental.pallas import tpu as pltpu
from jax.sharding import Mesh, PartitionSpec as P


def sparse_partial(gathered, tiles, cols, counts, out_pos):
    n_blocks, slots, side, _ = tiles.shape
    width = gathered.shape[1]
    n_src = gathered.shape[0]

    def kernel(cols_ref, counts_ref, tile_ref, src_ref, out_ref, acc_ref):
        b = pl.program_id(0)
        live = counts_ref[b]
        acc_ref[...] = jnp.zeros_like(acc_ref)
        for k in range(slots):
            @pl.when(k < live)
            def _():
                start = pl.multiple_of(cols_ref[b * slots + k] * side, side)
                src = src_ref[pl.ds(start, side), :]
                acc_ref[...] += jnp.dot(tile_ref[0, k], src, preferred_element_type=jnp.float32)
        out_ref[...] = acc_ref[...].astype(out_ref.dtype)

    grid_spec = pltpu.PrefetchScalarGridSpec(
        num_scalar_prefetch=2,
        grid=(n_blocks,),
        in_specs=[
            pl.BlockSpec((1, slots, side, side), lambda b, c, n: (b, 0, 0, 0)),
            pl.BlockSpec((n_src, width), lambda b, c, n: (0, 0)),
        ],
        out_specs=pl.BlockSpec((side, width), lambda b, c, n: (out_pos(b), 0)),
        scratch_shapes=[pltpu.VMEM((side, width), jnp.float32)],
    )
    return pl.pallas_call(
        kernel,
        grid_spec=grid_spec,
        out_shape=jax.ShapeDtypeStruct((n_blocks * side, width), jnp.bfloat16),
        compiler_params=pltpu.CompilerParams(
            dimension_semantics=("arbitrary",), vmem_limit_bytes=48 * 1024 * 1024
        ),
    )(cols.reshape(-1), counts, tiles, gathered)


N_CHUNKS = 4


def body(features, weight, bias, tile_vals, tile_col, tile_count):
    n_hi = lax.axis_size("yh")
    n_lo = lax.axis_size("z")
    per_dev = features.shape[0] // tile_vals.shape[-1]

    def out_pos(b):
        j = b // per_dev
        return ((j % n_lo) * n_hi + j // n_lo) * per_dev + b % per_dev

    n_rep = lax.axis_size("rep")
    width = features.shape[1]
    chunk = width // N_CHUNKS
    pieces = []
    for i in range(N_CHUNKS):
        cols = features[:, i * chunk:(i + 1) * chunk]
        copies = jnp.broadcast_to(cols[None], (n_rep,) + cols.shape).reshape(-1, chunk)
        gathered = lax.all_to_all(copies, "rep", 0, 0, tiled=True)
        partial = sparse_partial(gathered, tile_vals[0, 0], tile_col[0, 0], tile_count[0, 0], out_pos)
        part = lax.psum_scatter(partial, "z", scatter_dimension=0, tiled=True)
        pieces.append(lax.psum_scatter(part, "yh", scatter_dimension=0, tiled=True))
    summed = jnp.concatenate(pieces, axis=1)
    mixed = jnp.dot(summed, weight, preferred_element_type=jnp.float32) + bias.astype(jnp.float32)
    return jnp.maximum(mixed, 0.0).astype(jnp.bfloat16)


def solution(mesh):
    n_rep, n_blk = mesh.devices.shape
    n_hi = 2
    split = Mesh(mesh.devices.reshape(n_rep, n_hi, n_blk // n_hi), ("rep", "yh", "z"))
    blk = ("yh", "z")
    return jax.shard_map(
        body,
        mesh=split,
        in_specs=(
            P(("rep",) + blk, None),
            P(),
            P(),
            P("rep", blk, None, None, None, None),
            P("rep", blk, None, None),
            P("rep", blk, None),
        ),
        out_specs=P(("rep",) + blk, None),
        check_vma=False,
    )
```

```python
import jax
import jax.numpy as jnp
from jax import lax
from jax.experimental import pallas as pl
from jax.experimental.pallas import tpu as pltpu
from jax.sharding import Mesh, PartitionSpec as P


def sparse_partial(gathered, tiles, cols, counts, out_pos):
    n_blocks, slots, side, _ = tiles.shape
    width = gathered.shape[1]
    n_src = gathered.shape[0]

    def kernel(cols_ref, counts_ref, tile_ref, src_ref, out_ref, acc_ref):
        b = pl.program_id(0)
        live = counts_ref[b]
        acc_ref[...] = jnp.zeros_like(acc_ref)
        for k in range(slots):
            @pl.when(k < live)
            def _():
                start = pl.multiple_of(cols_ref[b * slots + k] * side, side)
                src = src_ref[pl.ds(start, side), :]
                acc_ref[...] += jnp.dot(tile_ref[0, k], src, preferred_element_type=jnp.float32)
        out_ref[...] = acc_ref[...].astype(out_ref.dtype)

    grid_spec = pltpu.PrefetchScalarGridSpec(
        num_scalar_prefetch=2,
        grid=(n_blocks,),
        in_specs=[
            pl.BlockSpec((1, slots, side, side), lambda b, c, n: (b, 0, 0, 0)),
            pl.BlockSpec((n_src, width), lambda b, c, n: (0, 0)),
        ],
        out_specs=pl.BlockSpec((side, width), lambda b, c, n: (out_pos(b), 0)),
        scratch_shapes=[pltpu.VMEM((side, width), jnp.float32)],
    )
    return pl.pallas_call(
        kernel,
        grid_spec=grid_spec,
        out_shape=jax.ShapeDtypeStruct((n_blocks * side, width), jnp.bfloat16),
        compiler_params=pltpu.CompilerParams(
            dimension_semantics=("arbitrary",), vmem_limit_bytes=48 * 1024 * 1024
        ),
    )(cols.reshape(-1), counts, tiles, gathered)


def body(features, weight, bias, tile_vals, tile_col, tile_count):
    n_hi = lax.axis_size("yh")
    n_lo = lax.axis_size("z")
    per_dev = features.shape[0] // tile_vals.shape[-1]

    def out_pos(b):
        j = b // per_dev
        return ((j % n_lo) * n_hi + j // n_lo) * per_dev + b % per_dev

    gathered = lax.all_gather(features, "rep", axis=0, tiled=True)
    partial = sparse_partial(gathered, tile_vals[0, 0], tile_col[0, 0], tile_count[0, 0], out_pos)
    summed = lax.psum_scatter(partial, "z", scatter_dimension=0, tiled=True)
    hi = lax.axis_index("yh")
    rows = summed.shape[0] // n_hi
    mine = lax.dynamic_slice_in_dim(summed, hi * rows, rows, axis=0)
    theirs = lax.dynamic_slice_in_dim(summed, (1 - hi) * rows, rows, axis=0)
    got = lax.ppermute(theirs, "yh", [(0, 1), (1, 0)])
    summed = (mine.astype(jnp.float32) + got.astype(jnp.float32)).astype(jnp.bfloat16)
    mixed = jnp.dot(summed, weight, preferred_element_type=jnp.float32) + bias.astype(jnp.float32)
    return jnp.maximum(mixed, 0.0).astype(jnp.bfloat16)


def solution(mesh):
    n_rep, n_blk = mesh.devices.shape
    n_hi = 2
    split = Mesh(mesh.devices.reshape(n_rep, n_hi, n_blk // n_hi), ("rep", "yh", "z"))
    blk = ("yh", "z")
    return jax.shard_map(
        body,
        mesh=split,
        in_specs=(
            P(("rep",) + blk, None),
            P(),
            P(),
            P("rep", blk, None, None, None, None),
            P("rep", blk, None, None),
            P("rep", blk, None),
        ),
        out_specs=P(("rep",) + blk, None),
        check_vma=False,
    )
```

```python
import jax
import jax.numpy as jnp
from jax import lax
from jax.experimental import pallas as pl
from jax.experimental.pallas import tpu as pltpu
from jax.sharding import Mesh, PartitionSpec as P


def sparse_partial(gathered, tiles, cols, counts, n_steps, block_of, out_pos):
    n_blocks, slots, side, _ = tiles.shape
    width = gathered.shape[1]
    n_src = gathered.shape[0]

    def kernel(cols_ref, counts_ref, tile_ref, src_ref, out_ref, acc_ref):
        b = block_of(pl.program_id(0))
        live = counts_ref[b]
        acc_ref[...] = jnp.zeros_like(acc_ref)
        for k in range(slots):
            @pl.when(k < live)
            def _():
                start = pl.multiple_of(cols_ref[b * slots + k] * side, side)
                src = src_ref[pl.ds(start, side), :]
                acc_ref[...] += jnp.dot(tile_ref[0, k], src, preferred_element_type=jnp.float32)
        out_ref[...] = acc_ref[...].astype(out_ref.dtype)

    grid_spec = pltpu.PrefetchScalarGridSpec(
        num_scalar_prefetch=2,
        grid=(n_steps,),
        in_specs=[
            pl.BlockSpec((1, slots, side, side), lambda i, c, n: (block_of(i), 0, 0, 0)),
            pl.BlockSpec((n_src, width), lambda b, c, n: (0, 0)),
        ],
        out_specs=pl.BlockSpec((side, width), lambda b, c, n: (out_pos(b), 0)),
        scratch_shapes=[pltpu.VMEM((side, width), jnp.float32)],
    )
    return pl.pallas_call(
        kernel,
        grid_spec=grid_spec,
        out_shape=jax.ShapeDtypeStruct((n_steps * side, width), jnp.bfloat16),
        compiler_params=pltpu.CompilerParams(
            dimension_semantics=("arbitrary",), vmem_limit_bytes=48 * 1024 * 1024
        ),
    )(cols.reshape(-1), counts, tiles, gathered)


def body(features, weight, bias, tile_vals, tile_col, tile_count):
    n_hi = lax.axis_size("yh")
    n_lo = lax.axis_size("z")
    side = tile_vals.shape[-1]
    per_dev = features.shape[0] // side
    n_dest = n_hi * n_lo
    hi = lax.axis_index("yh")

    gathered = lax.all_gather(features, "rep", axis=0, tiled=True)
    outs = []
    for sub in range(per_dev):
        def block_of(i, sub=sub):
            return i * per_dev + sub

        def out_pos(i):
            return (i % n_lo) * n_hi + i // n_lo

        partial = sparse_partial(
            gathered, tile_vals[0, 0], tile_col[0, 0], tile_count[0, 0], n_dest, block_of, out_pos
        )
        part = lax.psum_scatter(partial, "z", scatter_dimension=0, tiled=True)
        mine = lax.dynamic_slice_in_dim(part, hi * side, side, axis=0)
        theirs = lax.dynamic_slice_in_dim(part, (1 - hi) * side, side, axis=0)
        got = lax.ppermute(theirs, "yh", [(0, 1), (1, 0)])
        outs.append((mine.astype(jnp.float32) + got.astype(jnp.float32)).astype(jnp.bfloat16))
    summed = jnp.concatenate(outs, axis=0)
    mixed = jnp.dot(summed, weight, preferred_element_type=jnp.float32) + bias.astype(jnp.float32)
    return jnp.maximum(mixed, 0.0).astype(jnp.bfloat16)


def solution(mesh):
    n_rep, n_blk = mesh.devices.shape
    n_hi = 2
    split = Mesh(mesh.devices.reshape(n_rep, n_hi, n_blk // n_hi), ("rep", "yh", "z"))
    blk = ("yh", "z")
    return jax.shard_map(
        body,
        mesh=split,
        in_specs=(
            P(("rep",) + blk, None),
            P(),
            P(),
            P("rep", blk, None, None, None, None),
            P("rep", blk, None, None),
            P("rep", blk, None),
        ),
        out_specs=P(("rep",) + blk, None),
        check_vma=False,
    )
```

```python
import jax
import jax.numpy as jnp
from jax import lax
from jax.experimental import pallas as pl
from jax.experimental.pallas import tpu as pltpu
from jax.sharding import Mesh, PartitionSpec as P


def sparse_partial(gathered, tiles, cols, counts, out_pos, src_pos):
    n_blocks, slots, side, _ = tiles.shape
    width = gathered.shape[1]
    n_src = gathered.shape[0]

    def kernel(cols_ref, counts_ref, tile_ref, src_ref, out_ref, acc_ref):
        b = pl.program_id(0)
        live = counts_ref[b]
        acc_ref[...] = jnp.zeros_like(acc_ref)
        for k in range(slots):
            @pl.when(k < live)
            def _():
                start = pl.multiple_of(src_pos(cols_ref[b * slots + k]) * side, side)
                src = src_ref[pl.ds(start, side), :]
                acc_ref[...] += jnp.dot(tile_ref[0, k], src, preferred_element_type=jnp.float32)
        out_ref[...] = acc_ref[...].astype(out_ref.dtype)

    grid_spec = pltpu.PrefetchScalarGridSpec(
        num_scalar_prefetch=2,
        grid=(n_blocks,),
        in_specs=[
            pl.BlockSpec((1, slots, side, side), lambda b, c, n: (b, 0, 0, 0)),
            pl.BlockSpec((n_src, width), lambda b, c, n: (0, 0)),
        ],
        out_specs=pl.BlockSpec((side, width), lambda b, c, n: (out_pos(b), 0)),
        scratch_shapes=[pltpu.VMEM((side, width), jnp.float32)],
    )
    return pl.pallas_call(
        kernel,
        grid_spec=grid_spec,
        out_shape=jax.ShapeDtypeStruct((n_blocks * side, width), jnp.bfloat16),
        compiler_params=pltpu.CompilerParams(
            dimension_semantics=("arbitrary",), vmem_limit_bytes=48 * 1024 * 1024
        ),
    )(cols.reshape(-1), counts, tiles, gathered)


def body(features, weight, bias, tile_vals, tile_col, tile_count):
    n_hi = lax.axis_size("yh")
    n_lo = lax.axis_size("z")
    per_dev = features.shape[0] // tile_vals.shape[-1]

    def out_pos(b):
        j = b // per_dev
        return ((j % n_lo) * n_hi + j // n_lo) * per_dev + b % per_dev

    n_xy = lax.axis_size("rxy")
    n_core = lax.axis_size("core")

    def src_pos(c):
        r = c // per_dev
        return ((r % n_core) * n_xy + r // n_core) * per_dev + c % per_dev

    gathered = lax.all_gather(features, "rxy", axis=0, tiled=True)
    gathered = lax.all_gather(gathered, "core", axis=0, tiled=True)
    partial = sparse_partial(gathered, tile_vals[0, 0], tile_col[0, 0], tile_count[0, 0], out_pos, src_pos)
    summed = lax.psum_scatter(partial, "z", scatter_dimension=0, tiled=True)
    hi = lax.axis_index("yh")
    rows = summed.shape[0] // n_hi
    mine = lax.dynamic_slice_in_dim(summed, hi * rows, rows, axis=0)
    theirs = lax.dynamic_slice_in_dim(summed, (1 - hi) * rows, rows, axis=0)
    got = lax.ppermute(theirs, "yh", [(0, 1), (1, 0)])
    summed = (mine.astype(jnp.float32) + got.astype(jnp.float32)).astype(jnp.bfloat16)
    mixed = jnp.dot(summed, weight, preferred_element_type=jnp.float32) + bias.astype(jnp.float32)
    return jnp.maximum(mixed, 0.0).astype(jnp.bfloat16)


def solution(mesh):
    n_rep, n_blk = mesh.devices.shape
    n_hi = 2
    n_core = 2
    split = Mesh(
        mesh.devices.reshape(n_rep // n_core, n_core, n_hi, n_blk // n_hi), ("rxy", "core", "yh", "z")
    )
    rep = ("rxy", "core")
    blk = ("yh", "z")
    return jax.shard_map(
        body,
        mesh=split,
        in_specs=(
            P(rep + blk, None),
            P(),
            P(),
            P(rep, blk, None, None, None, None),
            P(rep, blk, None, None),
            P(rep, blk, None),
        ),
        out_specs=P(rep + blk, None),
        check_vma=False,
    )
```

```python
import jax
import jax.numpy as jnp
from jax import lax
from jax.experimental import pallas as pl
from jax.experimental.pallas import tpu as pltpu
from jax.sharding import Mesh, PartitionSpec as P


def sparse_partial(gathered, tiles, cols, counts, out_pos, group=2):
    n_blocks, slots, side, _ = tiles.shape
    width = gathered.shape[1]
    n_src = gathered.shape[0]

    def kernel(cols_ref, counts_ref, tile_ref, src_ref, out_ref):
        step = pl.program_id(0)
        for g in range(group):
            b = step * group + g
            live = counts_ref[b]
            lhs = jnp.concatenate(
                [jnp.where(k < live, tile_ref[g, k], jnp.zeros_like(tile_ref[g, k])) for k in range(slots)],
                axis=1,
            )
            rhs = jnp.concatenate(
                [
                    src_ref[pl.ds(pl.multiple_of(cols_ref[b * slots + k] * side, side), side), :]
                    for k in range(slots)
                ],
                axis=0,
            )
            out_ref[pl.ds(g * side, side), :] = jnp.dot(
                lhs, rhs, preferred_element_type=jnp.float32
            ).astype(out_ref.dtype)

    grid_spec = pltpu.PrefetchScalarGridSpec(
        num_scalar_prefetch=2,
        grid=(n_blocks // group,),
        in_specs=[
            pl.BlockSpec((group, slots, side, side), lambda i, c, n: (i, 0, 0, 0)),
            pl.BlockSpec((n_src, width), lambda i, c, n: (0, 0)),
        ],
        out_specs=pl.BlockSpec((group * side, width), lambda i, c, n: (out_pos(i * group) // group, 0)),
    )
    return pl.pallas_call(
        kernel,
        grid_spec=grid_spec,
        out_shape=jax.ShapeDtypeStruct((n_blocks * side, width), jnp.bfloat16),
        compiler_params=pltpu.CompilerParams(
            dimension_semantics=("arbitrary",), vmem_limit_bytes=48 * 1024 * 1024
        ),
    )(cols.reshape(-1), counts, tiles, gathered)


def body(features, weight, bias, tile_vals, tile_col, tile_count):
    n_hi = lax.axis_size("yh")
    n_lo = lax.axis_size("z")
    per_dev = features.shape[0] // tile_vals.shape[-1]

    def out_pos(b):
        j = b // per_dev
        return ((j % n_lo) * n_hi + j // n_lo) * per_dev + b % per_dev

    gathered = lax.all_gather(features, "rep", axis=0, tiled=True)
    partial = sparse_partial(gathered, tile_vals[0, 0], tile_col[0, 0], tile_count[0, 0], out_pos, per_dev)
    summed = lax.psum_scatter(partial, "z", scatter_dimension=0, tiled=True)
    hi = lax.axis_index("yh")
    rows = summed.shape[0] // n_hi
    mine = lax.dynamic_slice_in_dim(summed, hi * rows, rows, axis=0)
    theirs = lax.dynamic_slice_in_dim(summed, (1 - hi) * rows, rows, axis=0)
    got = lax.ppermute(theirs, "yh", [(0, 1), (1, 0)])
    summed = (mine.astype(jnp.float32) + got.astype(jnp.float32)).astype(jnp.bfloat16)
    mixed = jnp.dot(summed, weight, preferred_element_type=jnp.float32) + bias.astype(jnp.float32)
    return jnp.maximum(mixed, 0.0).astype(jnp.bfloat16)


def solution(mesh):
    n_rep, n_blk = mesh.devices.shape
    n_hi = 2
    split = Mesh(mesh.devices.reshape(n_rep, n_hi, n_blk // n_hi), ("rep", "yh", "z"))
    blk = ("yh", "z")
    return jax.shard_map(
        body,
        mesh=split,
        in_specs=(
            P(("rep",) + blk, None),
            P(),
            P(),
            P("rep", blk, None, None, None, None),
            P("rep", blk, None, None),
            P("rep", blk, None),
        ),
        out_specs=P(("rep",) + blk, None),
        check_vma=False,
    )
```

```python
import jax
import jax.numpy as jnp
from jax import lax
from jax.experimental import pallas as pl
from jax.experimental.pallas import tpu as pltpu
from jax.sharding import Mesh, PartitionSpec as P


def sparse_partial(gathered, tiles, cols, counts, out_pos, group=2):
    n_blocks, slots, side, _ = tiles.shape
    width = gathered.shape[1]
    n_src = gathered.shape[0]

    def kernel(cols_ref, counts_ref, tile_ref, src_ref, out_ref):
        step = pl.program_id(0)
        for g in range(group):
            b = step * group + g
            live = counts_ref[b]
            rows = pl.ds(g * side, side)
            for n in range(slots + 1):
                @pl.when(live == n)
                def _(n=n, b=b, g=g, rows=rows):
                    if n == 0:
                        out_ref[rows, :] = jnp.zeros((side, width), out_ref.dtype)
                        return
                    lhs = jnp.concatenate([tile_ref[g, k] for k in range(n)], axis=1)
                    rhs = jnp.concatenate(
                        [
                            src_ref[pl.ds(pl.multiple_of(cols_ref[b * slots + k] * side, side), side), :]
                            for k in range(n)
                        ],
                        axis=0,
                    )
                    out_ref[rows, :] = jnp.dot(lhs, rhs, preferred_element_type=jnp.float32).astype(
                        out_ref.dtype
                    )

    grid_spec = pltpu.PrefetchScalarGridSpec(
        num_scalar_prefetch=2,
        grid=(n_blocks // group,),
        in_specs=[
            pl.BlockSpec((group, slots, side, side), lambda i, c, n: (i, 0, 0, 0)),
            pl.BlockSpec((n_src, width), lambda i, c, n: (0, 0)),
        ],
        out_specs=pl.BlockSpec((group * side, width), lambda i, c, n: (out_pos(i * group) // group, 0)),
    )
    return pl.pallas_call(
        kernel,
        grid_spec=grid_spec,
        out_shape=jax.ShapeDtypeStruct((n_blocks * side, width), jnp.bfloat16),
        compiler_params=pltpu.CompilerParams(
            dimension_semantics=("arbitrary",), vmem_limit_bytes=48 * 1024 * 1024
        ),
    )(cols.reshape(-1), counts, tiles, gathered)


def body(features, weight, bias, tile_vals, tile_col, tile_count):
    n_hi = lax.axis_size("yh")
    n_lo = lax.axis_size("z")
    per_dev = features.shape[0] // tile_vals.shape[-1]

    def out_pos(b):
        j = b // per_dev
        return ((j % n_lo) * n_hi + j // n_lo) * per_dev + b % per_dev

    gathered = lax.all_gather(features, "rep", axis=0, tiled=True)
    partial = sparse_partial(gathered, tile_vals[0, 0], tile_col[0, 0], tile_count[0, 0], out_pos, per_dev)
    summed = lax.psum_scatter(partial, "z", scatter_dimension=0, tiled=True)
    hi = lax.axis_index("yh")
    rows = summed.shape[0] // n_hi
    mine = lax.dynamic_slice_in_dim(summed, hi * rows, rows, axis=0)
    theirs = lax.dynamic_slice_in_dim(summed, (1 - hi) * rows, rows, axis=0)
    got = lax.ppermute(theirs, "yh", [(0, 1), (1, 0)])
    summed = (mine.astype(jnp.float32) + got.astype(jnp.float32)).astype(jnp.bfloat16)
    mixed = jnp.dot(summed, weight, preferred_element_type=jnp.float32) + bias.astype(jnp.float32)
    return jnp.maximum(mixed, 0.0).astype(jnp.bfloat16)


def solution(mesh):
    n_rep, n_blk = mesh.devices.shape
    n_hi = 2
    split = Mesh(mesh.devices.reshape(n_rep, n_hi, n_blk // n_hi), ("rep", "yh", "z"))
    blk = ("yh", "z")
    return jax.shard_map(
        body,
        mesh=split,
        in_specs=(
            P(("rep",) + blk, None),
            P(),
            P(),
            P("rep", blk, None, None, None, None),
            P("rep", blk, None, None),
            P("rep", blk, None),
        ),
        out_specs=P(("rep",) + blk, None),
        check_vma=False,
    )
```

```python
import jax
import jax.numpy as jnp
from jax import lax
from jax.experimental import pallas as pl
from jax.experimental.pallas import tpu as pltpu
from jax.sharding import Mesh, PartitionSpec as P


def sparse_partial(gathered, tiles, cols, counts, out_pos, group=2):
    n_blocks, slots, side, _ = tiles.shape
    width = gathered.shape[1]
    n_src = gathered.shape[0]

    def kernel(cols_ref, counts_ref, tile_ref, src_ref, out_ref):
        step = pl.program_id(0)
        for g in range(group):
            b = step * group + g
            live = counts_ref[b]
            lhs = jnp.concatenate(
                [jnp.where(k < live, tile_ref[g, k], jnp.zeros_like(tile_ref[g, k])) for k in range(slots)],
                axis=1,
            )
            rhs = jnp.concatenate(
                [
                    src_ref[pl.ds(pl.multiple_of(cols_ref[b * slots + k] * side, side), side), :]
                    for k in range(slots)
                ],
                axis=0,
            )
            out_ref[pl.ds(g * side, side), :] = jnp.dot(
                lhs, rhs, preferred_element_type=jnp.float32
            ).astype(out_ref.dtype)

    grid_spec = pltpu.PrefetchScalarGridSpec(
        num_scalar_prefetch=2,
        grid=(n_blocks // group,),
        in_specs=[
            pl.BlockSpec((group, slots, side, side), lambda i, c, n: (i, 0, 0, 0)),
            pl.BlockSpec((n_src, width), lambda i, c, n: (0, 0)),
        ],
        out_specs=pl.BlockSpec((group * side, width), lambda i, c, n: (out_pos(i * group) // group, 0)),
    )
    return pl.pallas_call(
        kernel,
        grid_spec=grid_spec,
        out_shape=jax.ShapeDtypeStruct((n_blocks * side, width), jnp.bfloat16),
        compiler_params=pltpu.CompilerParams(
            dimension_semantics=("arbitrary",), vmem_limit_bytes=48 * 1024 * 1024
        ),
    )(cols.reshape(-1), counts, tiles, gathered)


N_SWAP = 4


def body(features, weight, bias, tile_vals, tile_col, tile_count):
    n_hi = lax.axis_size("yh")
    n_lo = lax.axis_size("z")
    per_dev = features.shape[0] // tile_vals.shape[-1]

    def out_pos(b):
        j = b // per_dev
        return ((j % n_lo) * n_hi + j // n_lo) * per_dev + b % per_dev

    gathered = lax.all_gather(features, "rep", axis=0, tiled=True)
    partial = sparse_partial(gathered, tile_vals[0, 0], tile_col[0, 0], tile_count[0, 0], out_pos, per_dev)
    summed = lax.psum_scatter(partial, "z", scatter_dimension=0, tiled=True)
    hi = lax.axis_index("yh")
    rows = summed.shape[0] // n_hi
    mine = lax.dynamic_slice_in_dim(summed, hi * rows, rows, axis=0)
    theirs = lax.dynamic_slice_in_dim(summed, (1 - hi) * rows, rows, axis=0)
    quarter = theirs.shape[1] // N_SWAP
    got = jnp.concatenate(
        [
            lax.ppermute(theirs[:, q * quarter:(q + 1) * quarter], "yh", [(0, 1), (1, 0)])
            for q in range(N_SWAP)
        ],
        axis=1,
    )
    summed = (mine.astype(jnp.float32) + got.astype(jnp.float32)).astype(jnp.bfloat16)
    mixed = jnp.dot(summed, weight, preferred_element_type=jnp.float32) + bias.astype(jnp.float32)
    return jnp.maximum(mixed, 0.0).astype(jnp.bfloat16)


def solution(mesh):
    n_rep, n_blk = mesh.devices.shape
    n_hi = 2
    split = Mesh(mesh.devices.reshape(n_rep, n_hi, n_blk // n_hi), ("rep", "yh", "z"))
    blk = ("yh", "z")
    return jax.shard_map(
        body,
        mesh=split,
        in_specs=(
            P(("rep",) + blk, None),
            P(),
            P(),
            P("rep", blk, None, None, None, None),
            P("rep", blk, None, None),
            P("rep", blk, None),
        ),
        out_specs=P(("rep",) + blk, None),
        check_vma=False,
    )
```

```python
import jax
import jax.numpy as jnp
from jax import lax
from jax.experimental import pallas as pl
from jax.experimental.pallas import tpu as pltpu
from jax.sharding import Mesh, PartitionSpec as P


def sparse_partial(gathered, tiles, cols, counts, out_pos, group=2):
    n_blocks, slots, side, _ = tiles.shape
    width = gathered.shape[1]
    n_src = gathered.shape[0]
    half = width // 2

    def kernel(cols_ref, counts_ref, tile_ref, src_ref, out_a, out_b):
        step = pl.program_id(0)
        for g in range(group):
            b = step * group + g
            live = counts_ref[b]
            lhs = jnp.concatenate(
                [jnp.where(k < live, tile_ref[g, k], jnp.zeros_like(tile_ref[g, k])) for k in range(slots)],
                axis=1,
            )
            rhs = jnp.concatenate(
                [
                    src_ref[pl.ds(pl.multiple_of(cols_ref[b * slots + k] * side, side), side), :]
                    for k in range(slots)
                ],
                axis=0,
            )
            prod = jnp.dot(lhs, rhs, preferred_element_type=jnp.float32).astype(out_a.dtype)
            out_a[pl.ds(g * side, side), :] = prod[:, :half]
            out_b[pl.ds(g * side, side), :] = prod[:, half:]

    grid_spec = pltpu.PrefetchScalarGridSpec(
        num_scalar_prefetch=2,
        grid=(n_blocks // group,),
        in_specs=[
            pl.BlockSpec((group, slots, side, side), lambda i, c, n: (i, 0, 0, 0)),
            pl.BlockSpec((n_src, width), lambda i, c, n: (0, 0)),
        ],
        out_specs=[
            pl.BlockSpec((group * side, half), lambda i, c, n: (out_pos(i * group) // group, 0)),
            pl.BlockSpec((group * side, half), lambda i, c, n: (out_pos(i * group) // group, 0)),
        ],
    )
    return pl.pallas_call(
        kernel,
        grid_spec=grid_spec,
        out_shape=[jax.ShapeDtypeStruct((n_blocks * side, half), jnp.bfloat16)] * 2,
        compiler_params=pltpu.CompilerParams(
            dimension_semantics=("arbitrary",), vmem_limit_bytes=48 * 1024 * 1024
        ),
    )(cols.reshape(-1), counts, tiles, gathered)


def body(features, weight, bias, tile_vals, tile_col, tile_count):
    n_hi = lax.axis_size("yh")
    n_lo = lax.axis_size("z")
    per_dev = features.shape[0] // tile_vals.shape[-1]

    def out_pos(b):
        j = b // per_dev
        return ((j % n_lo) * n_hi + j // n_lo) * per_dev + b % per_dev

    gathered = lax.all_gather(features, "rep", axis=0, tiled=True)
    part_a, part_b = sparse_partial(
        gathered, tile_vals[0, 0], tile_col[0, 0], tile_count[0, 0], out_pos, per_dev
    )
    hi = lax.axis_index("yh")
    swap = [(0, 1), (1, 0)]
    grid_b = part_b.reshape(n_lo, n_hi, -1, part_b.shape[1])
    mine_b = lax.dynamic_index_in_dim(grid_b, hi, axis=1, keepdims=False)
    theirs_b = lax.dynamic_index_in_dim(grid_b, 1 - hi, axis=1, keepdims=False)
    got_b = lax.ppermute(theirs_b, "yh", swap)
    sum_b = (mine_b.astype(jnp.float32) + got_b.astype(jnp.float32)).astype(jnp.bfloat16)
    sum_b = sum_b.reshape(-1, part_b.shape[1])
    red_a = lax.psum_scatter(part_a, "z", scatter_dimension=0, tiled=True)
    rows = red_a.shape[0] // n_hi
    mine = lax.dynamic_slice_in_dim(red_a, hi * rows, rows, axis=0)
    theirs = lax.dynamic_slice_in_dim(red_a, (1 - hi) * rows, rows, axis=0)
    got = lax.ppermute(theirs, "yh", swap)
    out_a = (mine.astype(jnp.float32) + got.astype(jnp.float32)).astype(jnp.bfloat16)
    out_b = lax.psum_scatter(sum_b, "z", scatter_dimension=0, tiled=True)
    summed = jnp.concatenate([out_a, out_b], axis=1)
    mixed = jnp.dot(summed, weight, preferred_element_type=jnp.float32) + bias.astype(jnp.float32)
    return jnp.maximum(mixed, 0.0).astype(jnp.bfloat16)


def solution(mesh):
    n_rep, n_blk = mesh.devices.shape
    n_hi = 2
    split = Mesh(mesh.devices.reshape(n_rep, n_hi, n_blk // n_hi), ("rep", "yh", "z"))
    blk = ("yh", "z")
    return jax.shard_map(
        body,
        mesh=split,
        in_specs=(
            P(("rep",) + blk, None),
            P(),
            P(),
            P("rep", blk, None, None, None, None),
            P("rep", blk, None, None),
            P("rep", blk, None),
        ),
        out_specs=P(("rep",) + blk, None),
        check_vma=False,
    )
```

```python
import jax
import jax.numpy as jnp
from jax import lax
from jax.experimental import pallas as pl
from jax.experimental.pallas import tpu as pltpu
from jax.sharding import Mesh, PartitionSpec as P


def sparse_partial(gathered, tiles, cols, counts, hi, n_lo, out_pos, group=2):
    n_blocks, slots, side, _ = tiles.shape
    width = gathered.shape[1]
    n_src = gathered.shape[0]
    half = width // 2

    def dest(i, hi_ref):
        h = hi_ref[0]
        plane = jnp.where(i < n_lo, h, 1 - h)
        return plane * n_lo + i % n_lo

    def kernel(cols_ref, counts_ref, hi_ref, tile_ref, src_ref, out_a, out_bm, out_bt):
        step = pl.program_id(0)
        j = dest(step, hi_ref)
        for g in range(group):
            b = j * group + g
            live = counts_ref[b]
            lhs = jnp.concatenate(
                [jnp.where(k < live, tile_ref[g, k], jnp.zeros_like(tile_ref[g, k])) for k in range(slots)],
                axis=1,
            )
            rhs = jnp.concatenate(
                [
                    src_ref[pl.ds(pl.multiple_of(cols_ref[b * slots + k] * side, side), side), :]
                    for k in range(slots)
                ],
                axis=0,
            )
            prod = jnp.dot(lhs, rhs, preferred_element_type=jnp.float32).astype(out_a.dtype)
            rows = pl.ds(g * side, side)
            out_a[rows, :] = prod[:, :half]

            @pl.when(step < n_lo)
            def _():
                out_bm[rows, :] = prod[:, half:]

            @pl.when(step >= n_lo)
            def _():
                out_bt[rows, :] = prod[:, half:]

    grid_spec = pltpu.PrefetchScalarGridSpec(
        num_scalar_prefetch=3,
        grid=(n_blocks // group,),
        in_specs=[
            pl.BlockSpec((group, slots, side, side), lambda i, c, n, h: (dest(i, h), 0, 0, 0)),
            pl.BlockSpec((n_src, width), lambda i, c, n, h: (0, 0)),
        ],
        out_specs=[
            pl.BlockSpec((group * side, half), lambda i, c, n, h: (out_pos(dest(i, h) * group) // group, 0)),
            pl.BlockSpec((group * side, half), lambda i, c, n, h: (jnp.minimum(i, n_lo - 1), 0)),
            pl.BlockSpec((group * side, half), lambda i, c, n, h: (jnp.maximum(i - n_lo, 0), 0)),
        ],
    )
    return pl.pallas_call(
        kernel,
        grid_spec=grid_spec,
        out_shape=[
            jax.ShapeDtypeStruct((n_blocks * side, half), jnp.bfloat16),
            jax.ShapeDtypeStruct((n_blocks * side // 2, half), jnp.bfloat16),
            jax.ShapeDtypeStruct((n_blocks * side // 2, half), jnp.bfloat16),
        ],
        compiler_params=pltpu.CompilerParams(
            dimension_semantics=("arbitrary",), vmem_limit_bytes=48 * 1024 * 1024
        ),
    )(cols.reshape(-1), counts, hi.reshape(1), tiles, gathered)


def body(features, weight, bias, tile_vals, tile_col, tile_count):
    n_hi = lax.axis_size("yh")
    n_lo = lax.axis_size("z")
    per_dev = features.shape[0] // tile_vals.shape[-1]

    def out_pos(b):
        j = b // per_dev
        return ((j % n_lo) * n_hi + j // n_lo) * per_dev + b % per_dev

    gathered = lax.all_gather(features, "rep", axis=0, tiled=True)
    hi = lax.axis_index("yh")
    swap = [(0, 1), (1, 0)]
    part_a, mine_b, theirs_b = sparse_partial(
        gathered, tile_vals[0, 0], tile_col[0, 0], tile_count[0, 0], hi.astype(jnp.int32), n_lo, out_pos, per_dev
    )
    got_b = lax.ppermute(theirs_b, "yh", swap)
    sum_b = (mine_b.astype(jnp.float32) + got_b.astype(jnp.float32)).astype(jnp.bfloat16)
    red_a = lax.psum_scatter(part_a, "z", scatter_dimension=0, tiled=True)
    rows = red_a.shape[0] // n_hi
    mine = lax.dynamic_slice_in_dim(red_a, hi * rows, rows, axis=0)
    theirs = lax.dynamic_slice_in_dim(red_a, (1 - hi) * rows, rows, axis=0)
    got = lax.ppermute(theirs, "yh", swap)
    out_a = (mine.astype(jnp.float32) + got.astype(jnp.float32)).astype(jnp.bfloat16)
    out_b = lax.psum_scatter(sum_b, "z", scatter_dimension=0, tiled=True)
    summed = jnp.concatenate([out_a, out_b], axis=1)
    mixed = jnp.dot(summed, weight, preferred_element_type=jnp.float32) + bias.astype(jnp.float32)
    return jnp.maximum(mixed, 0.0).astype(jnp.bfloat16)


def solution(mesh):
    n_rep, n_blk = mesh.devices.shape
    n_hi = 2
    split = Mesh(mesh.devices.reshape(n_rep, n_hi, n_blk // n_hi), ("rep", "yh", "z"))
    blk = ("yh", "z")
    return jax.shard_map(
        body,
        mesh=split,
        in_specs=(
            P(("rep",) + blk, None),
            P(),
            P(),
            P("rep", blk, None, None, None, None),
            P("rep", blk, None, None),
            P("rep", blk, None),
        ),
        out_specs=P(("rep",) + blk, None),
        check_vma=False,
    )
```

```python
import jax
import jax.numpy as jnp
from jax import lax
from jax.experimental import pallas as pl
from jax.experimental.pallas import tpu as pltpu
from jax.sharding import Mesh, PartitionSpec as P


def sparse_partial(slab_a, slab_b, tiles, cols, counts, me, n_rep, out_pos, group=2):
    n_blocks, slots, side, _ = tiles.shape
    half = slab_a.shape[1]
    n_src = slab_a.shape[0]
    per_src = n_src // side // n_rep

    def kernel(cols_ref, counts_ref, me_ref, tile_ref, a_ref, b_ref, out_a, out_b):
        step = pl.program_id(0)
        d = me_ref[0]
        for g in range(group):
            b = step * group + g
            live = counts_ref[b]
            lhs = jnp.concatenate(
                [jnp.where(k < live, tile_ref[g, k], jnp.zeros_like(tile_ref[g, k])) for k in range(slots)],
                axis=1,
            )
            srcs = [cols_ref[b * slots + k] for k in range(slots)]
            rhs_a = jnp.concatenate(
                [a_ref[pl.ds(pl.multiple_of(c * side, side), side), :] for c in srcs], axis=0
            )
            pos_b = [((d - c // per_src + n_rep) % n_rep) * per_src + c % per_src for c in srcs]
            rhs_b = jnp.concatenate(
                [b_ref[pl.ds(pl.multiple_of(p * side, side), side), :] for p in pos_b], axis=0
            )
            rows = pl.ds(g * side, side)
            out_a[rows, :] = jnp.dot(lhs, rhs_a, preferred_element_type=jnp.float32).astype(out_a.dtype)
            out_b[rows, :] = jnp.dot(lhs, rhs_b, preferred_element_type=jnp.float32).astype(out_b.dtype)

    grid_spec = pltpu.PrefetchScalarGridSpec(
        num_scalar_prefetch=3,
        grid=(n_blocks // group,),
        in_specs=[
            pl.BlockSpec((group, slots, side, side), lambda i, c, n, m: (i, 0, 0, 0)),
            pl.BlockSpec((n_src, half), lambda i, c, n, m: (0, 0)),
            pl.BlockSpec((n_src, slab_b.shape[1]), lambda i, c, n, m: (0, 0)),
        ],
        out_specs=[
            pl.BlockSpec((group * side, half), lambda i, c, n, m: (out_pos(i * group) // group, 0)),
            pl.BlockSpec((group * side, slab_b.shape[1]), lambda i, c, n, m: (out_pos(i * group) // group, 0)),
        ],
    )
    return pl.pallas_call(
        kernel,
        grid_spec=grid_spec,
        out_shape=[
            jax.ShapeDtypeStruct((n_blocks * side, half), jnp.bfloat16),
            jax.ShapeDtypeStruct((n_blocks * side, slab_b.shape[1]), jnp.bfloat16),
        ],
        compiler_params=pltpu.CompilerParams(
            dimension_semantics=("arbitrary",), vmem_limit_bytes=48 * 1024 * 1024
        ),
    )(cols.reshape(-1), counts, me.reshape(1), tiles, slab_a, slab_b)


def body(features, weight, bias, tile_vals, tile_col, tile_count):
    n_hi = lax.axis_size("yh")
    n_lo = lax.axis_size("z")
    per_dev = features.shape[0] // tile_vals.shape[-1]

    def out_pos(b):
        j = b // per_dev
        return ((j % n_lo) * n_hi + j // n_lo) * per_dev + b % per_dev

    n_rep = lax.axis_size("rep")
    me = lax.axis_index("rep").astype(jnp.int32)
    half = features.shape[1] // 2
    slab_a = lax.all_gather(features[:, :half], "rep", axis=0, tiled=True)
    own_b = features[:, half:]
    pieces = [own_b] + [
        lax.ppermute(own_b, "rep", [(i, (i + shift) % n_rep) for i in range(n_rep)])
        for shift in range(1, n_rep)
    ]
    slab_b = jnp.concatenate(pieces, axis=0)
    part_a, part_b = sparse_partial(
        slab_a, slab_b, tile_vals[0, 0], tile_col[0, 0], tile_count[0, 0], me, n_rep, out_pos, per_dev
    )
    hi = lax.axis_index("yh")
    swap = [(0, 1), (1, 0)]
    grid_b = part_b.reshape(n_lo, n_hi, -1, part_b.shape[1])
    mine_b = lax.dynamic_index_in_dim(grid_b, hi, axis=1, keepdims=False)
    theirs_b = lax.dynamic_index_in_dim(grid_b, 1 - hi, axis=1, keepdims=False)
    got_b = lax.ppermute(theirs_b, "yh", swap)
    sum_b = (mine_b.astype(jnp.float32) + got_b.astype(jnp.float32)).astype(jnp.bfloat16)
    sum_b = sum_b.reshape(-1, part_b.shape[1])
    red_a = lax.psum_scatter(part_a, "z", scatter_dimension=0, tiled=True)
    rows = red_a.shape[0] // n_hi
    mine = lax.dynamic_slice_in_dim(red_a, hi * rows, rows, axis=0)
    theirs = lax.dynamic_slice_in_dim(red_a, (1 - hi) * rows, rows, axis=0)
    got = lax.ppermute(theirs, "yh", swap)
    out_a = (mine.astype(jnp.float32) + got.astype(jnp.float32)).astype(jnp.bfloat16)
    out_b = lax.psum_scatter(sum_b, "z", scatter_dimension=0, tiled=True)
    summed = jnp.concatenate([out_a, out_b], axis=1)
    mixed = jnp.dot(summed, weight, preferred_element_type=jnp.float32) + bias.astype(jnp.float32)
    return jnp.maximum(mixed, 0.0).astype(jnp.bfloat16)


def solution(mesh):
    n_rep, n_blk = mesh.devices.shape
    n_hi = 2
    split = Mesh(mesh.devices.reshape(n_rep, n_hi, n_blk // n_hi), ("rep", "yh", "z"))
    blk = ("yh", "z")
    return jax.shard_map(
        body,
        mesh=split,
        in_specs=(
            P(("rep",) + blk, None),
            P(),
            P(),
            P("rep", blk, None, None, None, None),
            P("rep", blk, None, None),
            P("rep", blk, None),
        ),
        out_specs=P(("rep",) + blk, None),
        check_vma=False,
    )
```

```python
import jax
import jax.numpy as jnp
from jax import lax
from jax.experimental import pallas as pl
from jax.experimental.pallas import tpu as pltpu
from jax.sharding import Mesh, PartitionSpec as P


def sparse_partial(gathered, tiles, cols, counts, out_pos, group=2):
    n_blocks, slots, side, _ = tiles.shape
    width = gathered.shape[1]
    n_src = gathered.shape[0]
    half = width // 2

    n_steps = n_blocks // group
    per_step = group * slots

    def kernel(cols_ref, counts_ref, tile_ref, src_hbm, out_a, out_b, buf, sem):
        step = pl.program_id(0)

        def copies(at, parity):
            return [
                pltpu.make_async_copy(
                    src_hbm.at[pl.ds(pl.multiple_of(cols_ref[at * per_step + q] * side, side), side), :],
                    buf.at[parity, q],
                    sem.at[parity, q],
                )
                for q in range(per_step)
            ]

        @pl.when(step == 0)
        def _():
            for cp in copies(0, 0):
                cp.start()

        @pl.when(step + 1 < n_steps)
        def _():
            for cp in copies(step + 1, (step + 1) % 2):
                cp.start()

        parity = step % 2
        for cp in copies(step, parity):
            cp.wait()
        for g in range(group):
            b = step * group + g
            live = counts_ref[b]
            lhs = jnp.concatenate(
                [jnp.where(k < live, tile_ref[g, k], jnp.zeros_like(tile_ref[g, k])) for k in range(slots)],
                axis=1,
            )
            rhs = jnp.concatenate([buf[parity, g * slots + k] for k in range(slots)], axis=0)
            prod = jnp.dot(lhs, rhs, preferred_element_type=jnp.float32).astype(out_a.dtype)
            out_a[pl.ds(g * side, side), :] = prod[:, :half]
            out_b[pl.ds(g * side, side), :] = prod[:, half:]

    grid_spec = pltpu.PrefetchScalarGridSpec(
        num_scalar_prefetch=2,
        grid=(n_blocks // group,),
        in_specs=[
            pl.BlockSpec((group, slots, side, side), lambda i, c, n: (i, 0, 0, 0)),
            pl.BlockSpec(memory_space=pl.ANY),
        ],
        out_specs=[
            pl.BlockSpec((group * side, half), lambda i, c, n: (out_pos(i * group) // group, 0)),
            pl.BlockSpec((group * side, half), lambda i, c, n: (out_pos(i * group) // group, 0)),
        ],
        scratch_shapes=[
            pltpu.VMEM((2, per_step, side, width), gathered.dtype),
            pltpu.SemaphoreType.DMA((2, per_step)),
        ],
    )
    return pl.pallas_call(
        kernel,
        grid_spec=grid_spec,
        out_shape=[jax.ShapeDtypeStruct((n_blocks * side, half), jnp.bfloat16)] * 2,
        compiler_params=pltpu.CompilerParams(
            dimension_semantics=("arbitrary",), vmem_limit_bytes=48 * 1024 * 1024
        ),
    )(cols.reshape(-1), counts, tiles, gathered)


def body(features, weight, bias, tile_vals, tile_col, tile_count):
    n_hi = lax.axis_size("yh")
    n_lo = lax.axis_size("z")
    per_dev = features.shape[0] // tile_vals.shape[-1]

    def out_pos(b):
        j = b // per_dev
        return ((j % n_lo) * n_hi + j // n_lo) * per_dev + b % per_dev

    gathered = lax.all_gather(features, "rep", axis=0, tiled=True)
    part_a, part_b = sparse_partial(
        gathered, tile_vals[0, 0], tile_col[0, 0], tile_count[0, 0], out_pos, per_dev
    )
    hi = lax.axis_index("yh")
    swap = [(0, 1), (1, 0)]
    grid_b = part_b.reshape(n_lo, n_hi, -1, part_b.shape[1])
    mine_b = lax.dynamic_index_in_dim(grid_b, hi, axis=1, keepdims=False)
    theirs_b = lax.dynamic_index_in_dim(grid_b, 1 - hi, axis=1, keepdims=False)
    got_b = lax.ppermute(theirs_b, "yh", swap)
    sum_b = (mine_b.astype(jnp.float32) + got_b.astype(jnp.float32)).astype(jnp.bfloat16)
    sum_b = sum_b.reshape(-1, part_b.shape[1])
    red_a = lax.psum_scatter(part_a, "z", scatter_dimension=0, tiled=True)
    rows = red_a.shape[0] // n_hi
    mine = lax.dynamic_slice_in_dim(red_a, hi * rows, rows, axis=0)
    theirs = lax.dynamic_slice_in_dim(red_a, (1 - hi) * rows, rows, axis=0)
    got = lax.ppermute(theirs, "yh", swap)
    out_a = (mine.astype(jnp.float32) + got.astype(jnp.float32)).astype(jnp.bfloat16)
    out_b = lax.psum_scatter(sum_b, "z", scatter_dimension=0, tiled=True)
    summed = jnp.concatenate([out_a, out_b], axis=1)
    mixed = jnp.dot(summed, weight, preferred_element_type=jnp.float32) + bias.astype(jnp.float32)
    return jnp.maximum(mixed, 0.0).astype(jnp.bfloat16)


def solution(mesh):
    n_rep, n_blk = mesh.devices.shape
    n_hi = 2
    split = Mesh(mesh.devices.reshape(n_rep, n_hi, n_blk // n_hi), ("rep", "yh", "z"))
    blk = ("yh", "z")
    return jax.shard_map(
        body,
        mesh=split,
        in_specs=(
            P(("rep",) + blk, None),
            P(),
            P(),
            P("rep", blk, None, None, None, None),
            P("rep", blk, None, None),
            P("rep", blk, None),
        ),
        out_specs=P(("rep",) + blk, None),
        check_vma=False,
    )
```

```python
import jax
import jax.numpy as jnp
from jax import lax
from jax.experimental import pallas as pl
from jax.experimental.pallas import tpu as pltpu
from jax.sharding import Mesh, PartitionSpec as P


def sparse_partial(gathered, tiles, cols, counts, out_pos, group=2):
    n_blocks, slots, side, _ = tiles.shape
    width = gathered.shape[1]
    n_src = gathered.shape[0]
    half = width // 2

    n_steps = n_blocks // group
    per_step = group * slots

    def kernel(cols_ref, counts_ref, tile_ref, src_hbm, out_a, out_b, buf, sem):
        step = pl.program_id(0)

        def copies(at, parity):
            return [
                (
                    q % slots < counts_ref[at * group + q // slots],
                    pltpu.make_async_copy(
                        src_hbm.at[pl.ds(pl.multiple_of(cols_ref[at * per_step + q] * side, side), side), :],
                        buf.at[parity, q],
                        sem.at[parity, q],
                    ),
                )
                for q in range(per_step)
            ]

        def start_all(at, parity):
            for live_q, cp in copies(at, parity):
                pl.when(live_q)(cp.start)

        @pl.when(step == 0)
        def _():
            start_all(0, 0)

        @pl.when(step + 1 < n_steps)
        def _():
            start_all(step + 1, (step + 1) % 2)

        parity = step % 2
        for live_q, cp in copies(step, parity):
            pl.when(live_q)(cp.wait)
        for g in range(group):
            b = step * group + g
            live = counts_ref[b]
            rows = pl.ds(g * side, side)
            for n in range(slots + 1):
                @pl.when(live == n)
                def _(n=n, g=g, rows=rows):
                    if n == 0:
                        out_a[rows, :] = jnp.zeros((side, half), out_a.dtype)
                        out_b[rows, :] = jnp.zeros((side, half), out_b.dtype)
                        return
                    lhs = jnp.concatenate([tile_ref[g, k] for k in range(n)], axis=1)
                    rhs = jnp.concatenate([buf[parity, g * slots + k] for k in range(n)], axis=0)
                    prod = jnp.dot(lhs, rhs, preferred_element_type=jnp.float32).astype(out_a.dtype)
                    out_a[rows, :] = prod[:, :half]
                    out_b[rows, :] = prod[:, half:]

    grid_spec = pltpu.PrefetchScalarGridSpec(
        num_scalar_prefetch=2,
        grid=(n_blocks // group,),
        in_specs=[
            pl.BlockSpec((group, slots, side, side), lambda i, c, n: (i, 0, 0, 0)),
            pl.BlockSpec(memory_space=pl.ANY),
        ],
        out_specs=[
            pl.BlockSpec((group * side, half), lambda i, c, n: (out_pos(i * group) // group, 0)),
            pl.BlockSpec((group * side, half), lambda i, c, n: (out_pos(i * group) // group, 0)),
        ],
        scratch_shapes=[
            pltpu.VMEM((2, per_step, side, width), gathered.dtype),
            pltpu.SemaphoreType.DMA((2, per_step)),
        ],
    )
    return pl.pallas_call(
        kernel,
        grid_spec=grid_spec,
        out_shape=[jax.ShapeDtypeStruct((n_blocks * side, half), jnp.bfloat16)] * 2,
        compiler_params=pltpu.CompilerParams(
            dimension_semantics=("arbitrary",), vmem_limit_bytes=48 * 1024 * 1024
        ),
    )(cols.reshape(-1), counts, tiles, gathered)


def body(features, weight, bias, tile_vals, tile_col, tile_count):
    n_hi = lax.axis_size("yh")
    n_lo = lax.axis_size("z")
    per_dev = features.shape[0] // tile_vals.shape[-1]

    def out_pos(b):
        j = b // per_dev
        return ((j % n_lo) * n_hi + j // n_lo) * per_dev + b % per_dev

    gathered = lax.all_gather(features, "rep", axis=0, tiled=True)
    part_a, part_b = sparse_partial(
        gathered, tile_vals[0, 0], tile_col[0, 0], tile_count[0, 0], out_pos, per_dev
    )
    hi = lax.axis_index("yh")
    swap = [(0, 1), (1, 0)]
    grid_b = part_b.reshape(n_lo, n_hi, -1, part_b.shape[1])
    mine_b = lax.dynamic_index_in_dim(grid_b, hi, axis=1, keepdims=False)
    theirs_b = lax.dynamic_index_in_dim(grid_b, 1 - hi, axis=1, keepdims=False)
    got_b = lax.ppermute(theirs_b, "yh", swap)
    sum_b = (mine_b.astype(jnp.float32) + got_b.astype(jnp.float32)).astype(jnp.bfloat16)
    sum_b = sum_b.reshape(-1, part_b.shape[1])
    red_a = lax.psum_scatter(part_a, "z", scatter_dimension=0, tiled=True)
    rows = red_a.shape[0] // n_hi
    mine = lax.dynamic_slice_in_dim(red_a, hi * rows, rows, axis=0)
    theirs = lax.dynamic_slice_in_dim(red_a, (1 - hi) * rows, rows, axis=0)
    got = lax.ppermute(theirs, "yh", swap)
    out_a = (mine.astype(jnp.float32) + got.astype(jnp.float32)).astype(jnp.bfloat16)
    out_b = lax.psum_scatter(sum_b, "z", scatter_dimension=0, tiled=True)
    summed = jnp.concatenate([out_a, out_b], axis=1)
    mixed = jnp.dot(summed, weight, preferred_element_type=jnp.float32) + bias.astype(jnp.float32)
    return jnp.maximum(mixed, 0.0).astype(jnp.bfloat16)


def solution(mesh):
    n_rep, n_blk = mesh.devices.shape
    n_hi = 2
    split = Mesh(mesh.devices.reshape(n_rep, n_hi, n_blk // n_hi), ("rep", "yh", "z"))
    blk = ("yh", "z")
    return jax.shard_map(
        body,
        mesh=split,
        in_specs=(
            P(("rep",) + blk, None),
            P(),
            P(),
            P("rep", blk, None, None, None, None),
            P("rep", blk, None, None),
            P("rep", blk, None),
        ),
        out_specs=P(("rep",) + blk, None),
        check_vma=False,
    )
```

```python
import jax
import jax.numpy as jnp
from jax import lax
from jax.experimental import pallas as pl
from jax.experimental.pallas import tpu as pltpu
from jax.sharding import Mesh, PartitionSpec as P


def sparse_partial(gathered, tiles, cols, counts, n_hi, n_lo, group=2):
    n_blocks, slots, side, _ = tiles.shape
    width = gathered.shape[1]
    n_src = gathered.shape[0]
    half = width // 2

    def kernel(cols_ref, counts_ref, *refs):
        tile_refs = refs[:n_hi]
        src_ref, out_a, out_b = refs[n_hi:]
        lo = pl.program_id(0)
        for hh in range(n_hi):
            for g in range(group):
                b = (hh * n_lo + lo) * group + g
                live = counts_ref[b]
                tref = tile_refs[hh]
                lhs = jnp.concatenate(
                    [jnp.where(k < live, tref[g, k], jnp.zeros_like(tref[g, k])) for k in range(slots)],
                    axis=1,
                )
                rhs = jnp.concatenate(
                    [
                        src_ref[pl.ds(pl.multiple_of(cols_ref[b * slots + k] * side, side), side), :]
                        for k in range(slots)
                    ],
                    axis=0,
                )
                prod = jnp.dot(lhs, rhs, preferred_element_type=jnp.float32).astype(out_a.dtype)
                rows = pl.ds((hh * group + g) * side, side)
                out_a[rows, :] = prod[:, :half]
                out_b[rows, :] = prod[:, half:]

    def tile_spec(hh):
        return pl.BlockSpec((group, slots, side, side), lambda i, c, n: (hh * n_lo + i, 0, 0, 0))

    grid_spec = pltpu.PrefetchScalarGridSpec(
        num_scalar_prefetch=2,
        grid=(n_lo,),
        in_specs=[tile_spec(hh) for hh in range(n_hi)] + [pl.BlockSpec((n_src, width), lambda i, c, n: (0, 0))],
        out_specs=[
            pl.BlockSpec((n_hi * group * side, half), lambda i, c, n: (i, 0)),
            pl.BlockSpec((n_hi * group * side, half), lambda i, c, n: (i, 0)),
        ],
    )
    return pl.pallas_call(
        kernel,
        grid_spec=grid_spec,
        out_shape=[jax.ShapeDtypeStruct((n_blocks * side, half), jnp.bfloat16)] * 2,
        compiler_params=pltpu.CompilerParams(
            dimension_semantics=("arbitrary",), vmem_limit_bytes=48 * 1024 * 1024
        ),
    )(cols.reshape(-1), counts, *([tiles] * n_hi), gathered)


def body(features, weight, bias, tile_vals, tile_col, tile_count):
    n_hi = lax.axis_size("yh")
    n_lo = lax.axis_size("z")
    per_dev = features.shape[0] // tile_vals.shape[-1]

    def out_pos(b):
        j = b // per_dev
        return ((j % n_lo) * n_hi + j // n_lo) * per_dev + b % per_dev

    gathered = lax.all_gather(features, "rep", axis=0, tiled=True)
    part_a, part_b = sparse_partial(
        gathered, tile_vals[0, 0], tile_col[0, 0], tile_count[0, 0], n_hi, n_lo, per_dev
    )
    hi = lax.axis_index("yh")
    swap = [(0, 1), (1, 0)]
    grid_b = part_b.reshape(n_lo, n_hi, -1, part_b.shape[1])
    mine_b = lax.dynamic_index_in_dim(grid_b, hi, axis=1, keepdims=False)
    theirs_b = lax.dynamic_index_in_dim(grid_b, 1 - hi, axis=1, keepdims=False)
    got_b = lax.ppermute(theirs_b, "yh", swap)
    sum_b = (mine_b.astype(jnp.float32) + got_b.astype(jnp.float32)).astype(jnp.bfloat16)
    sum_b = sum_b.reshape(-1, part_b.shape[1])
    red_a = lax.psum_scatter(part_a, "z", scatter_dimension=0, tiled=True)
    rows = red_a.shape[0] // n_hi
    mine = lax.dynamic_slice_in_dim(red_a, hi * rows, rows, axis=0)
    theirs = lax.dynamic_slice_in_dim(red_a, (1 - hi) * rows, rows, axis=0)
    got = lax.ppermute(theirs, "yh", swap)
    out_a = (mine.astype(jnp.float32) + got.astype(jnp.float32)).astype(jnp.bfloat16)
    out_b = lax.psum_scatter(sum_b, "z", scatter_dimension=0, tiled=True)
    summed = jnp.concatenate([out_a, out_b], axis=1)
    mixed = jnp.dot(summed, weight, preferred_element_type=jnp.float32) + bias.astype(jnp.float32)
    return jnp.maximum(mixed, 0.0).astype(jnp.bfloat16)


def solution(mesh):
    n_rep, n_blk = mesh.devices.shape
    n_hi = 2
    split = Mesh(mesh.devices.reshape(n_rep, n_hi, n_blk // n_hi), ("rep", "yh", "z"))
    blk = ("yh", "z")
    return jax.shard_map(
        body,
        mesh=split,
        in_specs=(
            P(("rep",) + blk, None),
            P(),
            P(),
            P("rep", blk, None, None, None, None),
            P("rep", blk, None, None),
            P("rep", blk, None),
        ),
        out_specs=P(("rep",) + blk, None),
        check_vma=False,
    )
```

```python
import jax
import jax.numpy as jnp
from jax import lax
from jax.experimental import pallas as pl
from jax.experimental.pallas import tpu as pltpu
from jax.sharding import Mesh, PartitionSpec as P


def sparse_partial(gathered, tiles, cols, counts, n_hi, n_lo, group=2, lo_step=2):
    n_blocks, slots, side, _ = tiles.shape
    width = gathered.shape[1]
    n_src = gathered.shape[0]
    half = width // 2

    def kernel(cols_ref, counts_ref, *refs):
        tile_refs = refs[: n_hi * lo_step]
        src_ref, out_a, out_b = refs[n_hi * lo_step:]
        step = pl.program_id(0)
        for l in range(lo_step):
          for hh in range(n_hi):
            for g in range(group):
                b = (hh * n_lo + step * lo_step + l) * group + g
                live = counts_ref[b]
                tref = tile_refs[l * n_hi + hh]
                lhs = jnp.concatenate(
                    [jnp.where(k < live, tref[g, k], jnp.zeros_like(tref[g, k])) for k in range(slots)],
                    axis=1,
                )
                rhs = jnp.concatenate(
                    [
                        src_ref[pl.ds(pl.multiple_of(cols_ref[b * slots + k] * side, side), side), :]
                        for k in range(slots)
                    ],
                    axis=0,
                )
                prod = jnp.dot(lhs, rhs, preferred_element_type=jnp.float32).astype(out_a.dtype)
                rows = pl.ds(((l * n_hi + hh) * group + g) * side, side)
                out_a[rows, :] = prod[:, :half]
                out_b[rows, :] = prod[:, half:]

    def tile_spec(l, hh):
        return pl.BlockSpec((group, slots, side, side), lambda i, c, n: (hh * n_lo + i * lo_step + l, 0, 0, 0))

    grid_spec = pltpu.PrefetchScalarGridSpec(
        num_scalar_prefetch=2,
        grid=(n_lo // lo_step,),
        in_specs=[tile_spec(l, hh) for l in range(lo_step) for hh in range(n_hi)] + [pl.BlockSpec((n_src, width), lambda i, c, n: (0, 0))],
        out_specs=[
            pl.BlockSpec((lo_step * n_hi * group * side, half), lambda i, c, n: (i, 0)),
            pl.BlockSpec((lo_step * n_hi * group * side, half), lambda i, c, n: (i, 0)),
        ],
    )
    return pl.pallas_call(
        kernel,
        grid_spec=grid_spec,
        out_shape=[jax.ShapeDtypeStruct((n_blocks * side, half), jnp.bfloat16)] * 2,
        compiler_params=pltpu.CompilerParams(
            dimension_semantics=("arbitrary",), vmem_limit_bytes=48 * 1024 * 1024
        ),
    )(cols.reshape(-1), counts, *([tiles] * (n_hi * lo_step)), gathered)


def body(features, weight, bias, tile_vals, tile_col, tile_count):
    n_hi = lax.axis_size("yh")
    n_lo = lax.axis_size("z")
    per_dev = features.shape[0] // tile_vals.shape[-1]

    def out_pos(b):
        j = b // per_dev
        return ((j % n_lo) * n_hi + j // n_lo) * per_dev + b % per_dev

    gathered = lax.all_gather(features, "rep", axis=0, tiled=True)
    part_a, part_b = sparse_partial(
        gathered, tile_vals[0, 0], tile_col[0, 0], tile_count[0, 0], n_hi, n_lo, per_dev
    )
    hi = lax.axis_index("yh")
    swap = [(0, 1), (1, 0)]
    grid_b = part_b.reshape(n_lo, n_hi, -1, part_b.shape[1])
    mine_b = lax.dynamic_index_in_dim(grid_b, hi, axis=1, keepdims=False)
    theirs_b = lax.dynamic_index_in_dim(grid_b, 1 - hi, axis=1, keepdims=False)
    got_b = lax.ppermute(theirs_b, "yh", swap)
    sum_b = (mine_b.astype(jnp.float32) + got_b.astype(jnp.float32)).astype(jnp.bfloat16)
    sum_b = sum_b.reshape(-1, part_b.shape[1])
    red_a = lax.psum_scatter(part_a, "z", scatter_dimension=0, tiled=True)
    rows = red_a.shape[0] // n_hi
    mine = lax.dynamic_slice_in_dim(red_a, hi * rows, rows, axis=0)
    theirs = lax.dynamic_slice_in_dim(red_a, (1 - hi) * rows, rows, axis=0)
    got = lax.ppermute(theirs, "yh", swap)
    out_a = (mine.astype(jnp.float32) + got.astype(jnp.float32)).astype(jnp.bfloat16)
    out_b = lax.psum_scatter(sum_b, "z", scatter_dimension=0, tiled=True)
    summed = jnp.concatenate([out_a, out_b], axis=1)
    mixed = jnp.dot(summed, weight, preferred_element_type=jnp.float32) + bias.astype(jnp.float32)
    return jnp.maximum(mixed, 0.0).astype(jnp.bfloat16)


def solution(mesh):
    n_rep, n_blk = mesh.devices.shape
    n_hi = 2
    split = Mesh(mesh.devices.reshape(n_rep, n_hi, n_blk // n_hi), ("rep", "yh", "z"))
    blk = ("yh", "z")
    return jax.shard_map(
        body,
        mesh=split,
        in_specs=(
            P(("rep",) + blk, None),
            P(),
            P(),
            P("rep", blk, None, None, None, None),
            P("rep", blk, None, None),
            P("rep", blk, None),
        ),
        out_specs=P(("rep",) + blk, None),
        check_vma=False,
    )
```

```python
import jax
import jax.numpy as jnp
from jax import lax
from jax.experimental import pallas as pl
from jax.experimental.pallas import tpu as pltpu
from jax.sharding import Mesh, PartitionSpec as P


def sparse_partial(gathered, tiles, cols, counts, n_hi, n_lo, group=2, lo_step=4):
    n_blocks, slots, side, _ = tiles.shape
    width = gathered.shape[1]
    n_src = gathered.shape[0]
    half = width // 2

    def kernel(cols_ref, counts_ref, *refs):
        tile_refs = refs[: n_hi * lo_step]
        src_ref, out_a, out_b = refs[n_hi * lo_step:]
        step = pl.program_id(0)
        for l in range(lo_step):
          for hh in range(n_hi):
            for g in range(group):
                b = (hh * n_lo + step * lo_step + l) * group + g
                live = counts_ref[b]
                tref = tile_refs[l * n_hi + hh]
                lhs = jnp.concatenate(
                    [jnp.where(k < live, tref[g, k], jnp.zeros_like(tref[g, k])) for k in range(slots)],
                    axis=1,
                )
                rhs = jnp.concatenate(
                    [
                        src_ref[pl.ds(pl.multiple_of(cols_ref[b * slots + k] * side, side), side), :]
                        for k in range(slots)
                    ],
                    axis=0,
                )
                prod = jnp.dot(lhs, rhs, preferred_element_type=jnp.float32).astype(out_a.dtype)
                rows = pl.ds(((l * n_hi + hh) * group + g) * side, side)
                out_a[rows, :] = prod[:, :half]
                out_b[rows, :] = prod[:, half:]

    def tile_spec(l, hh):
        return pl.BlockSpec((group, slots, side, side), lambda i, c, n: (hh * n_lo + i * lo_step + l, 0, 0, 0))

    grid_spec = pltpu.PrefetchScalarGridSpec(
        num_scalar_prefetch=2,
        grid=(n_lo // lo_step,),
        in_specs=[tile_spec(l, hh) for l in range(lo_step) for hh in range(n_hi)] + [pl.BlockSpec((n_src, width), lambda i, c, n: (0, 0))],
        out_specs=[
            pl.BlockSpec((lo_step * n_hi * group * side, half), lambda i, c, n: (i, 0)),
            pl.BlockSpec((lo_step * n_hi * group * side, half), lambda i, c, n: (i, 0)),
        ],
    )
    return pl.pallas_call(
        kernel,
        grid_spec=grid_spec,
        out_shape=[jax.ShapeDtypeStruct((n_blocks * side, half), jnp.bfloat16)] * 2,
        compiler_params=pltpu.CompilerParams(
            dimension_semantics=("arbitrary",), vmem_limit_bytes=48 * 1024 * 1024
        ),
    )(cols.reshape(-1), counts, *([tiles] * (n_hi * lo_step)), gathered)


def body(features, weight, bias, tile_vals, tile_col, tile_count):
    n_hi = lax.axis_size("yh")
    n_lo = lax.axis_size("z")
    per_dev = features.shape[0] // tile_vals.shape[-1]

    def out_pos(b):
        j = b // per_dev
        return ((j % n_lo) * n_hi + j // n_lo) * per_dev + b % per_dev

    gathered = lax.all_gather(features, "rep", axis=0, tiled=True)
    part_a, part_b = sparse_partial(
        gathered, tile_vals[0, 0], tile_col[0, 0], tile_count[0, 0], n_hi, n_lo, per_dev
    )
    hi = lax.axis_index("yh")
    swap = [(0, 1), (1, 0)]
    grid_b = part_b.reshape(n_lo, n_hi, -1, part_b.shape[1])
    mine_b = lax.dynamic_index_in_dim(grid_b, hi, axis=1, keepdims=False)
    theirs_b = lax.dynamic_index_in_dim(grid_b, 1 - hi, axis=1, keepdims=False)
    got_b = lax.ppermute(theirs_b, "yh", swap)
    sum_b = (mine_b.astype(jnp.float32) + got_b.astype(jnp.float32)).astype(jnp.bfloat16)
    sum_b = sum_b.reshape(-1, part_b.shape[1])
    red_a = lax.psum_scatter(part_a, "z", scatter_dimension=0, tiled=True)
    rows = red_a.shape[0] // n_hi
    mine = lax.dynamic_slice_in_dim(red_a, hi * rows, rows, axis=0)
    theirs = lax.dynamic_slice_in_dim(red_a, (1 - hi) * rows, rows, axis=0)
    got = lax.ppermute(theirs, "yh", swap)
    out_a = (mine.astype(jnp.float32) + got.astype(jnp.float32)).astype(jnp.bfloat16)
    out_b = lax.psum_scatter(sum_b, "z", scatter_dimension=0, tiled=True)
    summed = jnp.concatenate([out_a, out_b], axis=1)
    mixed = jnp.dot(summed, weight, preferred_element_type=jnp.float32) + bias.astype(jnp.float32)
    return jnp.maximum(mixed, 0.0).astype(jnp.bfloat16)


def solution(mesh):
    n_rep, n_blk = mesh.devices.shape
    n_hi = 2
    split = Mesh(mesh.devices.reshape(n_rep, n_hi, n_blk // n_hi), ("rep", "yh", "z"))
    blk = ("yh", "z")
    return jax.shard_map(
        body,
        mesh=split,
        in_specs=(
            P(("rep",) + blk, None),
            P(),
            P(),
            P("rep", blk, None, None, None, None),
            P("rep", blk, None, None),
            P("rep", blk, None),
        ),
        out_specs=P(("rep",) + blk, None),
        check_vma=False,
    )
```

```python
import jax
import jax.numpy as jnp
from jax import lax
from jax.experimental import pallas as pl
from jax.experimental.pallas import tpu as pltpu
from jax.sharding import Mesh, PartitionSpec as P


def sparse_partial(gathered, tiles, cols, counts, n_hi, n_lo, group=2, lo_step=4):
    n_blocks, slots, side, _ = tiles.shape
    width = gathered.shape[1]
    n_src = gathered.shape[0]
    half = width // 2

    def kernel(cols_ref, counts_ref, *refs):
        tile_refs = refs[: n_hi * lo_step]
        src_ref, out_a, out_b = refs[n_hi * lo_step:]
        step = pl.program_id(0)
        for l in range(lo_step):
          for hh in range(n_hi):
            for g in range(group):
                b = (hh * n_lo + step * lo_step + l) * group + g
                live = counts_ref[b]
                tref = tile_refs[l * n_hi + hh]
                lhs = jnp.concatenate(
                    [jnp.where(k < live, tref[g, k], jnp.zeros_like(tref[g, k])) for k in range(slots)],
                    axis=1,
                )
                rhs = jnp.concatenate(
                    [
                        src_ref[pl.ds(pl.multiple_of(cols_ref[b * slots + k] * side, side), side), :]
                        for k in range(slots)
                    ],
                    axis=0,
                )
                prod = jnp.dot(lhs, rhs, preferred_element_type=jnp.float32).astype(out_a.dtype)
                rows = pl.ds(((l * n_hi + hh) * group + g) * side, side)
                out_a[rows, :] = prod[:, :half]
                out_b[rows, :] = prod[:, half:]

    def tile_spec(l, hh):
        return pl.BlockSpec((group, slots, side, side), lambda i, c, n: (hh * n_lo + i * lo_step + l, 0, 0, 0))

    grid_spec = pltpu.PrefetchScalarGridSpec(
        num_scalar_prefetch=2,
        grid=(n_lo // lo_step,),
        in_specs=[tile_spec(l, hh) for l in range(lo_step) for hh in range(n_hi)] + [pl.BlockSpec((n_src, width), lambda i, c, n: (0, 0))],
        out_specs=[
            pl.BlockSpec((lo_step * n_hi * group * side, half), lambda i, c, n: (i, 0)),
            pl.BlockSpec((lo_step * n_hi * group * side, half), lambda i, c, n: (i, 0)),
        ],
    )
    return pl.pallas_call(
        kernel,
        grid_spec=grid_spec,
        out_shape=[jax.ShapeDtypeStruct((n_blocks * side, half), jnp.bfloat16)] * 2,
        compiler_params=pltpu.CompilerParams(
            dimension_semantics=("arbitrary",), vmem_limit_bytes=48 * 1024 * 1024
        ),
    )(cols.reshape(-1), counts, *([tiles] * (n_hi * lo_step)), gathered)


def body(features, weight, bias, tile_vals, tile_col, tile_count):
    n_hi = lax.axis_size("yh")
    n_lo = lax.axis_size("z")
    per_dev = features.shape[0] // tile_vals.shape[-1]

    def out_pos(b):
        j = b // per_dev
        return ((j % n_lo) * n_hi + j // n_lo) * per_dev + b % per_dev

    gathered = lax.all_gather(features, "rep", axis=0, tiled=True)
    part_a, part_b = sparse_partial(
        gathered, tile_vals[0, 0], tile_col[0, 0], tile_count[0, 0], n_hi, n_lo, per_dev
    )
    hi = lax.axis_index("yh")
    swap = [(0, 1), (1, 0)]
    grid_b = part_b.reshape(n_lo, n_hi, -1, part_b.shape[1])
    mine_b = lax.dynamic_index_in_dim(grid_b, hi, axis=1, keepdims=False)
    theirs_b = lax.dynamic_index_in_dim(grid_b, 1 - hi, axis=1, keepdims=False)
    got_b = lax.ppermute(theirs_b, "yh", swap)
    sum_b = (mine_b.astype(jnp.float32) + got_b.astype(jnp.float32)).astype(jnp.bfloat16)
    sum_b = sum_b.reshape(-1, part_b.shape[1])
    red_a = lax.psum_scatter(part_a, "z", scatter_dimension=0, tiled=True)
    rows = red_a.shape[0] // n_hi
    mine = lax.dynamic_slice_in_dim(red_a, hi * rows, rows, axis=0)
    theirs = lax.dynamic_slice_in_dim(red_a, (1 - hi) * rows, rows, axis=0)
    got = lax.ppermute(theirs, "yh", swap)
    out_a = (mine.astype(jnp.float32) + got.astype(jnp.float32)).astype(jnp.bfloat16)
    out_b = lax.psum_scatter(sum_b, "z", scatter_dimension=0, tiled=True)
    cut = out_a.shape[1]
    mixed = jnp.dot(out_a, weight[:cut], preferred_element_type=jnp.float32) + bias.astype(jnp.float32)
    mixed = mixed + jnp.dot(out_b, weight[cut:], preferred_element_type=jnp.float32)
    return jnp.maximum(mixed, 0.0).astype(jnp.bfloat16)


def solution(mesh):
    n_rep, n_blk = mesh.devices.shape
    n_hi = 2
    split = Mesh(mesh.devices.reshape(n_rep, n_hi, n_blk // n_hi), ("rep", "yh", "z"))
    blk = ("yh", "z")
    return jax.shard_map(
        body,
        mesh=split,
        in_specs=(
            P(("rep",) + blk, None),
            P(),
            P(),
            P("rep", blk, None, None, None, None),
            P("rep", blk, None, None),
            P("rep", blk, None),
        ),
        out_specs=P(("rep",) + blk, None),
        check_vma=False,
    )
```

```python
import jax
import jax.numpy as jnp
from jax import lax
from jax.experimental import pallas as pl
from jax.experimental.pallas import tpu as pltpu
from jax.sharding import Mesh, PartitionSpec as P


def sparse_partial(gathered, tiles, cols, counts, n_hi, n_lo, group=2, lo_step=8):
    n_blocks, slots, side, _ = tiles.shape
    width = gathered.shape[1]
    n_src = gathered.shape[0]
    half = width // 2

    def kernel(cols_ref, counts_ref, *refs):
        tile_refs = refs[: n_hi * lo_step]
        src_ref, out_a, out_b = refs[n_hi * lo_step:]
        step = pl.program_id(0)
        for l in range(lo_step):
          for hh in range(n_hi):
            for g in range(group):
                b = (hh * n_lo + step * lo_step + l) * group + g
                live = counts_ref[b]
                tref = tile_refs[l * n_hi + hh]
                lhs = jnp.concatenate(
                    [jnp.where(k < live, tref[g, k], jnp.zeros_like(tref[g, k])) for k in range(slots)],
                    axis=1,
                )
                rhs = jnp.concatenate(
                    [
                        src_ref[pl.ds(pl.multiple_of(cols_ref[b * slots + k] * side, side), side), :]
                        for k in range(slots)
                    ],
                    axis=0,
                )
                prod = jnp.dot(lhs, rhs, preferred_element_type=jnp.float32).astype(out_a.dtype)
                rows = pl.ds(((l * n_hi + hh) * group + g) * side, side)
                out_a[rows, :] = prod[:, :half]
                out_b[rows, :] = prod[:, half:]

    def tile_spec(l, hh):
        return pl.BlockSpec((group, slots, side, side), lambda i, c, n: (hh * n_lo + i * lo_step + l, 0, 0, 0))

    grid_spec = pltpu.PrefetchScalarGridSpec(
        num_scalar_prefetch=2,
        grid=(n_lo // lo_step,),
        in_specs=[tile_spec(l, hh) for l in range(lo_step) for hh in range(n_hi)] + [pl.BlockSpec((n_src, width), lambda i, c, n: (0, 0))],
        out_specs=[
            pl.BlockSpec((lo_step * n_hi * group * side, half), lambda i, c, n: (i, 0)),
            pl.BlockSpec((lo_step * n_hi * group * side, half), lambda i, c, n: (i, 0)),
        ],
    )
    return pl.pallas_call(
        kernel,
        grid_spec=grid_spec,
        out_shape=[jax.ShapeDtypeStruct((n_blocks * side, half), jnp.bfloat16)] * 2,
        compiler_params=pltpu.CompilerParams(
            dimension_semantics=("arbitrary",), vmem_limit_bytes=48 * 1024 * 1024
        ),
    )(cols.reshape(-1), counts, *([tiles] * (n_hi * lo_step)), gathered)


def body(features, weight, bias, tile_vals, tile_col, tile_count):
    n_hi = lax.axis_size("yh")
    n_lo = lax.axis_size("z")
    per_dev = features.shape[0] // tile_vals.shape[-1]

    def out_pos(b):
        j = b // per_dev
        return ((j % n_lo) * n_hi + j // n_lo) * per_dev + b % per_dev

    gathered = lax.all_gather(features, "rep", axis=0, tiled=True)
    part_a, part_b = sparse_partial(
        gathered, tile_vals[0, 0], tile_col[0, 0], tile_count[0, 0], n_hi, n_lo, per_dev
    )
    hi = lax.axis_index("yh")
    swap = [(0, 1), (1, 0)]
    grid_b = part_b.reshape(n_lo, n_hi, -1, part_b.shape[1])
    mine_b = lax.dynamic_index_in_dim(grid_b, hi, axis=1, keepdims=False)
    theirs_b = lax.dynamic_index_in_dim(grid_b, 1 - hi, axis=1, keepdims=False)
    got_b = lax.ppermute(theirs_b, "yh", swap)
    sum_b = (mine_b.astype(jnp.float32) + got_b.astype(jnp.float32)).astype(jnp.bfloat16)
    sum_b = sum_b.reshape(-1, part_b.shape[1])
    red_a = lax.psum_scatter(part_a, "z", scatter_dimension=0, tiled=True)
    rows = red_a.shape[0] // n_hi
    mine = lax.dynamic_slice_in_dim(red_a, hi * rows, rows, axis=0)
    theirs = lax.dynamic_slice_in_dim(red_a, (1 - hi) * rows, rows, axis=0)
    got = lax.ppermute(theirs, "yh", swap)
    out_a = (mine.astype(jnp.float32) + got.astype(jnp.float32)).astype(jnp.bfloat16)
    out_b = lax.psum_scatter(sum_b, "z", scatter_dimension=0, tiled=True)
    summed = jnp.concatenate([out_a, out_b], axis=1)
    mixed = jnp.dot(summed, weight, preferred_element_type=jnp.float32) + bias.astype(jnp.float32)
    return jnp.maximum(mixed, 0.0).astype(jnp.bfloat16)


def solution(mesh):
    n_rep, n_blk = mesh.devices.shape
    n_hi = 2
    split = Mesh(mesh.devices.reshape(n_rep, n_hi, n_blk // n_hi), ("rep", "yh", "z"))
    blk = ("yh", "z")
    return jax.shard_map(
        body,
        mesh=split,
        in_specs=(
            P(("rep",) + blk, None),
            P(),
            P(),
            P("rep", blk, None, None, None, None),
            P("rep", blk, None, None),
            P("rep", blk, None),
        ),
        out_specs=P(("rep",) + blk, None),
        check_vma=False,
    )
```
